32 devices in a mesh: shot: 8 (over z, y), rcv: 4 (over x, core).
Axes of the slice: x: 2, y: 2, z: 4, core: 2. Of those that a mesh axis runs over, the one named last changes fastest.
Arguments:
- records: bfloat16 [1, 2, 1024, 8192], P(None, None, 'shot', 'rcv'), may hold values from -6 to 6
- aperture: int32 [1024, 2], P('shot'), may hold values from 0 to 3, all different within a row
- block_owner: int32 [4], replicated, may hold values from 0 to 7, as said below
- block_receivers: int32 [4, 128], replicated, may hold values from 0 to 8191, as said below
Outputs:
- multiples: bfloat16 [1, 2, 1024, 8192], P(None, None, 'shot', 'rcv')
The draws below stay inside these ranges and needn't reach their ends.
Inputs may be any that keep to these rules, and one draw needn't show every extreme that they name: `block_owner`: distinct indices. `block_receivers`: distinct receivers.
All inputs are finite; a program needn't handle non-finite values.
Results may differ from the reference program's by a relative error of at most 0.001.
Values may be sent and summed in bfloat16 or wider, within the bound.
No kernel may reach another device: no remote copies, remote signals or barrier semaphores. Data moves between devices by JAX's collectives and lax.ppermute only.
A program may use at most 128 MiB of HBM per device.

```python
import jax
import jax.numpy as jnp
from jax import lax

F = 1
SH_DEV = 128
RCV = 8192
NBLK = 4
APER = 2
BLOCK = 128
SHOTS = 1024
N_SHOT = 8


def draw_block_owner(key, part):
    middle = jax.random.permutation(jax.random.fold_in(key, 11), N_SHOT - 2)[:NBLK - 2] + 1
    ends = jnp.array([0, N_SHOT - 1], dtype=jnp.int32)
    owners = jnp.concatenate([ends, middle.astype(jnp.int32)])
    placing = jax.random.permutation(jax.random.fold_in(key, 13), NBLK)
    return owners[placing].astype(jnp.int32)


def draw_block_receivers(key, part):
    middle = jax.random.permutation(jax.random.fold_in(key, 23), RCV - 2)[:NBLK * BLOCK - 2] + 1
    ends = jnp.array([0, RCV - 1], dtype=jnp.int32)
    chosen = jnp.concatenate([ends, middle.astype(jnp.int32)])
    placing = jax.random.permutation(jax.random.fold_in(key, 29), NBLK * BLOCK)
    return chosen[placing].reshape(NBLK, BLOCK).astype(jnp.int32)


def levels(key, extent, shards, smallest, high):
    factor_of = 1.0
    for position, shards_of in shards:
        heights = jax.random.uniform(jax.random.fold_in(jax.random.fold_in(key, 6), position), (shards_of,), jnp.float32, smallest / len(shards), high / len(shards))
        factor_of = factor_of * jnp.repeat(jnp.exp(heights), extent[position] // shards_of).reshape((-1,) + (1,) * (len(extent) - 1 - position))
    return factor_of


def different_ones(key, rows, amount, top, lift):
    order = jax.random.permutation(jax.random.fold_in(key, 1), amount)
    pull = order
    for power in range(3):
        pull = pull * pull // amount
    pull = pull * lift // amount
    chance = jax.random.randint(jax.random.fold_in(key, 2), (rows, amount), 0, 4096) + pull
    sure = jax.random.permutation(jax.random.fold_in(key, 3), rows)[jnp.arange(amount) % rows]
    chance = jnp.where(jnp.arange(rows)[:, None] == sure[None, :], 1 << 14, chance)
    score = chance * amount + jnp.arange(amount)
    return lax.top_k(score.astype(jnp.int32), top)[1].astype(jnp.int32)


def gaussian(key, extent, scale, limit, cuts=(), kind=jnp.bfloat16):
    values = scale * jax.random.normal(key, extent, jnp.float32)
    if cuts:
        values = values * levels(key, extent, cuts, -0.22, 0.18)
    return jnp.clip(values, -limit, limit).astype(kind)


def setup_inputs(seed: int = 0) -> dict:
    seeds = jax.random.split(jax.random.key(seed), 5)
    records = gaussian(seeds[0], (F, 2, SHOTS, RCV), 1.0, 6.0, ((2, 8), (3, 4)))
    aperture = different_ones(seeds[1], SHOTS, NBLK, APER, 8192)
    block_owner = draw_block_owner(jax.random.fold_in(seeds[4], 71), 0)
    block_receivers = draw_block_receivers(jax.random.fold_in(seeds[4], 71), 0)
    return {"records": records, "aperture": aperture, "block_owner": block_owner, "block_receivers": block_receivers}


def reference(records, aperture, block_owner, block_receivers):
    cols = block_receivers.reshape(-1).astype(jnp.int32)
    near = jnp.take(records, cols, axis=3)
    blocks = jnp.arange(NBLK, dtype=jnp.int32)
    use = jnp.any(aperture[:, :, None] == blocks[None, None, :], axis=1)
    near = near.reshape(F, 2, SHOTS, NBLK, BLOCK) * use[None, None, :, :, None].astype(near.dtype)
    near = near.reshape(F, 2, SHOTS, NBLK * BLOCK).astype(jnp.float32)
    real_total = jnp.zeros((F, SHOTS, RCV), jnp.float32)
    imaginary_total = jnp.zeros((F, SHOTS, RCV), jnp.float32)
    for block in range(NBLK):
        start = (block_owner[block] * SH_DEV).astype(jnp.int32)
        distant_offset = lax.dynamic_slice_in_dim(records, start, SH_DEV, axis=2).astype(jnp.float32)
        block_portion = near[:, :, :, block * BLOCK:(block + 1) * BLOCK]
        real_total = real_total + jnp.einsum('uze,uew->uzw', block_portion[:, 0], distant_offset[:, 0]) - jnp.einsum('uze,uew->uzw', block_portion[:, 1], distant_offset[:, 1])
        imaginary_total = imaginary_total + jnp.einsum('uze,uew->uzw', block_portion[:, 0], distant_offset[:, 1]) + jnp.einsum('uze,uew->uzw', block_portion[:, 1], distant_offset[:, 0])
    factor = (2.0 * APER * BLOCK) ** -0.5
    return (jnp.stack([real_total, imaginary_total], axis=1) * factor).astype(jnp.bfloat16)
```

```python
import jax
import jax.numpy as jnp
from jax import lax
from jax.sharding import PartitionSpec as P

APER = 2
BLOCK = 128


def ring_order(n):
    if n % 2:
        return list(range(n))
    return list(range(0, n, 2)) + list(range(n - 1, 0, -2))


def local_columns(records, block_receivers):
    rcv_here = records.shape[3]
    first_rcv = lax.axis_index("rcv") * rcv_here
    requested = block_receivers.reshape(1, -1)
    column_ids = first_rcv + lax.broadcasted_iota(jnp.int32, (rcv_here, 1), 0)
    selector = (column_ids == requested).astype(jnp.bfloat16)
    picked = jnp.einsum("fcsr,rx->fcsx", records, selector, preferred_element_type=jnp.float32)
    return picked.astype(jnp.bfloat16)


def gather_near(picked, n_rcv):
    total = picked.astype(jnp.float32)
    for k in range(1, n_rcv):
        moved = lax.ppermute(picked, "rcv", [(i, (i + k) % n_rcv) for i in range(n_rcv)])
        total = total + moved.astype(jnp.float32)
    return total.astype(jnp.bfloat16)


def piece_product(lhs, piece):
    nblk, freqs, parts, extent, width = piece.shape
    rhs = piece.transpose(1, 2, 0, 3, 4).reshape(freqs, parts * nblk * extent, width)
    return jnp.einsum("fsk,fkw->fsw", lhs, rhs, preferred_element_type=jnp.float32)


def per_device(records, aperture, block_owner, block_receivers, n_shot, n_rcv):
    freqs, parts, shots_here, rcv_here = records.shape
    nblocks, block_extent = block_receivers.shape
    width = rcv_here // n_shot

    picked = local_columns(records, block_receivers)
    near = gather_near(picked, n_rcv)
    blocks = lax.broadcasted_iota(jnp.int32, (1, 1, nblocks), 2)
    use = jnp.any(aperture[:, :, None] == blocks, axis=1).astype(jnp.bfloat16)
    masked = near.reshape(freqs, parts, shots_here, nblocks, block_extent) * use[None, None, :, :, None]
    masked = masked.reshape(freqs, parts, shots_here, nblocks * block_extent)
    nr, ni = masked[:, 0], masked[:, 1]
    lhs = jnp.concatenate(
        [jnp.concatenate([nr, -ni], axis=2), jnp.concatenate([ni, nr], axis=2)], axis=1
    )

    pieces = records.reshape(freqs, parts, shots_here, n_shot, width).transpose(3, 0, 1, 2, 4)
    pieces = lax.all_to_all(pieces, "shot", 0, 0, tiled=True)
    mine = jnp.take(pieces, block_owner, axis=0)

    order = ring_order(n_shot)
    where = [0] * n_shot
    for k, d in enumerate(order):
        where[d] = k
    order_arr = jnp.array(order, jnp.int32)
    me = lax.axis_index("shot")
    pos = jnp.array(where, jnp.int32)[me]
    forward = [(order[k], order[(k + 1) % n_shot]) for k in range(n_shot)]
    backward = [(order[k], order[(k - 1) % n_shot]) for k in range(n_shot)]
    n_fwd = n_shot // 2
    n_bwd = n_shot - 1 - n_fwd

    outs = [piece_product(lhs, mine)]
    came_from = [me]
    fwd, bwd = mine, mine
    for t in range(1, max(n_fwd, n_bwd) + 1):
        if t <= n_fwd:
            fwd = lax.ppermute(fwd, "shot", forward)
            outs.append(piece_product(lhs, fwd))
            came_from.append(order_arr[(pos - t) % n_shot])
        if t <= n_bwd:
            bwd = lax.ppermute(bwd, "shot", backward)
            outs.append(piece_product(lhs, bwd))
            came_from.append(order_arr[(pos + t) % n_shot])
    came_from = jnp.stack(came_from)
    arrival = jnp.zeros((n_shot,), jnp.int32).at[came_from].set(jnp.arange(n_shot, dtype=jnp.int32))
    stacked = jnp.take(jnp.stack(outs), arrival, axis=0)
    factor = (2.0 * APER * BLOCK) ** (-0.5)
    total = (stacked * factor).astype(jnp.bfloat16)
    total = total.reshape(n_shot, freqs, parts, shots_here, width).transpose(1, 2, 3, 0, 4)
    return total.reshape(freqs, parts, shots_here, rcv_here)


def solution(mesh):
    n_shot = mesh.shape["shot"]
    n_rcv = mesh.shape["rcv"]
    placed = (P(None, None, "shot", "rcv"), P("shot", None), P(), P())

    def body(records, aperture, block_owner, block_receivers):
        return per_device(records, aperture, block_owner, block_receivers, n_shot, n_rcv)

    return jax.shard_map(
        body,
        mesh=mesh,
        in_specs=placed,
        out_specs=P(None, None, "shot", "rcv"),
        check_vma=False,
    )
```

```python
import jax
import jax.numpy as jnp
from jax import lax
from jax.sharding import PartitionSpec as P

APER = 2
BLOCK = 128


def ring_order(n):
    if n % 2:
        return list(range(n))
    return list(range(0, n, 2)) + list(range(n - 1, 0, -2))


def local_columns(records, block_receivers):
    rcv_here = records.shape[3]
    first_rcv = lax.axis_index("rcv") * rcv_here
    requested = block_receivers.reshape(1, -1)
    column_ids = first_rcv + lax.broadcasted_iota(jnp.int32, (rcv_here, 1), 0)
    selector = (column_ids == requested).astype(jnp.bfloat16)
    picked = jnp.einsum("fcsr,rx->fcsx", records, selector, preferred_element_type=jnp.float32)
    return picked.astype(jnp.bfloat16)


def gather_near(picked, n_rcv):
    total = picked.astype(jnp.float32)
    for k in range(1, n_rcv):
        moved = lax.ppermute(picked, "rcv", [(i, (i + k) % n_rcv) for i in range(n_rcv)])
        total = total + moved.astype(jnp.float32)
    return total.astype(jnp.bfloat16)


def piece_product(lhs, piece):
    nblk, freqs, parts, extent, width = piece.shape
    rhs = piece.transpose(1, 2, 0, 3, 4).reshape(freqs, parts * nblk * extent, width)
    return jnp.einsum("fsk,fkw->fsw", lhs, rhs, preferred_element_type=jnp.float32)


def per_device(records, aperture, block_owner, block_receivers, n_shot, n_rcv):
    freqs, parts, shots_here, rcv_here = records.shape
    nblocks, block_extent = block_receivers.shape
    width = rcv_here // n_shot

    picked = local_columns(records, block_receivers)
    near = gather_near(picked, n_rcv)
    blocks = lax.broadcasted_iota(jnp.int32, (1, 1, nblocks), 2)
    use = jnp.any(aperture[:, :, None] == blocks, axis=1).astype(jnp.bfloat16)
    masked = near.reshape(freqs, parts, shots_here, nblocks, block_extent) * use[None, None, :, :, None]
    masked = masked.reshape(freqs, parts, shots_here, nblocks * block_extent)
    nr, ni = masked[:, 0], masked[:, 1]
    lhs = jnp.concatenate(
        [jnp.concatenate([nr, -ni], axis=2), jnp.concatenate([ni, nr], axis=2)], axis=1
    )

    pieces = lax.all_to_all(records, "shot", 3, 0, tiled=True)
    pieces = pieces.reshape(n_shot, freqs, parts, shots_here, width)
    mine = jnp.take(pieces, block_owner, axis=0)

    order = ring_order(n_shot)
    where = [0] * n_shot
    for k, d in enumerate(order):
        where[d] = k
    order_arr = jnp.array(order, jnp.int32)
    me = lax.axis_index("shot")
    pos = jnp.array(where, jnp.int32)[me]
    forward = [(order[k], order[(k + 1) % n_shot]) for k in range(n_shot)]
    backward = [(order[k], order[(k - 1) % n_shot]) for k in range(n_shot)]
    n_fwd = n_shot // 2
    n_bwd = n_shot - 1 - n_fwd
    split_last = n_fwd > n_bwd and width % 2 == 0
    half = width // 2

    factor = (2.0 * APER * BLOCK) ** (-0.5)
    total = jnp.zeros((freqs, parts * shots_here, rcv_here), jnp.bfloat16)

    def place(total, piece, source):
        product = (piece_product(lhs, piece) * factor).astype(jnp.bfloat16)
        return lax.dynamic_update_slice_in_dim(total, product, source * width, axis=2)

    total = place(total, mine, me)
    fwd, bwd = mine, mine
    for t in range(1, max(n_fwd, n_bwd) + 1):
        if t == n_fwd and split_last:
            first = lax.ppermute(fwd[..., :half], "shot", forward)
            second = lax.ppermute(bwd[..., half:], "shot", backward)
            total = place(total, jnp.concatenate([first, second], axis=-1), order_arr[(pos - t) % n_shot])
            continue
        if t <= n_fwd:
            fwd = lax.ppermute(fwd, "shot", forward)
            total = place(total, fwd, order_arr[(pos - t) % n_shot])
        if t <= n_bwd:
            bwd = lax.ppermute(bwd, "shot", backward)
            total = place(total, bwd, order_arr[(pos + t) % n_shot])
    return total.reshape(freqs, parts, shots_here, rcv_here)


def solution(mesh):
    n_shot = mesh.shape["shot"]
    n_rcv = mesh.shape["rcv"]
    placed = (P(None, None, "shot", "rcv"), P("shot", None), P(), P())

    def body(records, aperture, block_owner, block_receivers):
        return per_device(records, aperture, block_owner, block_receivers, n_shot, n_rcv)

    return jax.shard_map(
        body,
        mesh=mesh,
        in_specs=placed,
        out_specs=P(None, None, "shot", "rcv"),
        check_vma=False,
    )
```

```python
import jax
import jax.numpy as jnp
from jax import lax
from jax.sharding import PartitionSpec as P

APER = 2
BLOCK = 128


def ring_order(n):
    if n % 2:
        return list(range(n))
    return list(range(0, n, 2)) + list(range(n - 1, 0, -2))


def local_columns(records, block_receivers):
    rcv_here = records.shape[3]
    first_rcv = lax.axis_index("rcv") * rcv_here
    requested = block_receivers.reshape(1, -1)
    column_ids = first_rcv + lax.broadcasted_iota(jnp.int32, (rcv_here, 1), 0)
    selector = (column_ids == requested).astype(jnp.bfloat16)
    picked = jnp.einsum("fcsr,rx->fcsx", records, selector, preferred_element_type=jnp.float32)
    return picked.astype(jnp.bfloat16)


def gather_near(picked, n_rcv):
    total = picked.astype(jnp.float32)
    for k in range(1, n_rcv):
        moved = lax.ppermute(picked, "rcv", [(i, (i + k) % n_rcv) for i in range(n_rcv)])
        total = total + moved.astype(jnp.float32)
    return total.astype(jnp.bfloat16)


def piece_product(lhs, piece):
    nblk, freqs, parts, extent, width = piece.shape
    rhs = piece.transpose(1, 2, 0, 3, 4).reshape(freqs, parts * nblk * extent, width)
    return jnp.einsum("fsk,fkw->fsw", lhs, rhs, preferred_element_type=jnp.float32)


def per_device(records, aperture, block_owner, block_receivers, n_shot, n_rcv):
    freqs, parts, shots_here, rcv_here = records.shape
    nblocks, block_extent = block_receivers.shape

    picked = local_columns(records, block_receivers)
    near = gather_near(picked, n_rcv)
    blocks = lax.broadcasted_iota(jnp.int32, (1, 1, nblocks), 2)
    use = jnp.any(aperture[:, :, None] == blocks, axis=1).astype(jnp.bfloat16)
    masked = near.reshape(freqs, parts, shots_here, nblocks, block_extent) * use[None, None, :, :, None]
    masked = masked.reshape(freqs, parts, shots_here, nblocks * block_extent)
    nr, ni = masked[:, 0], masked[:, 1]
    lhs = jnp.concatenate(
        [jnp.concatenate([nr, -ni], axis=2), jnp.concatenate([ni, nr], axis=2)], axis=1
    )

    order = ring_order(n_shot)
    where = [0] * n_shot
    for k, d in enumerate(order):
        where[d] = k
    order_arr = jnp.array(order, jnp.int32)
    me = lax.axis_index("shot")
    pos = jnp.array(where, jnp.int32)[me]
    forward = [(order[k], order[(k + 1) % n_shot]) for k in range(n_shot)]
    backward = [(order[k], order[(k - 1) % n_shot]) for k in range(n_shot)]
    n_fwd = n_shot // 2
    n_bwd = n_shot - 1 - n_fwd

    rows = shots_here // n_shot
    split_last = n_fwd > n_bwd and rcv_here % 2 == 0
    half = rcv_here // 2
    nk = lhs.shape[2]
    lhs_rows = lhs.reshape(freqs, 2 * shots_here, nk // block_extent, block_extent)

    def add(total, piece, source):
        part = lax.dynamic_slice_in_dim(lhs_rows, source * rows, rows, axis=3)
        part = part.reshape(freqs, 2 * shots_here, -1)
        rhs = piece.transpose(1, 2, 0, 3, 4).reshape(freqs, -1, rcv_here)
        return total + jnp.einsum("fsk,fkw->fsw", part, rhs, preferred_element_type=jnp.float32)

    pieces = lax.all_to_all(records, "shot", 2, 0, tiled=True)
    pieces = pieces.reshape(n_shot, freqs, parts, rows, rcv_here)
    mine = jnp.take(pieces, block_owner, axis=0)

    total = add(jnp.zeros((freqs, 2 * shots_here, rcv_here), jnp.float32), mine, me)
    fwd, bwd = mine, mine
    for t in range(1, max(n_fwd, n_bwd) + 1):
        if t == n_fwd and split_last:
            first = lax.ppermute(fwd[..., :half], "shot", forward)
            second = lax.ppermute(bwd[..., half:], "shot", backward)
            joined = jnp.concatenate([first, second], axis=-1)
            total = add(total, joined, order_arr[(pos - t) % n_shot])
            continue
        if t <= n_fwd:
            fwd = lax.ppermute(fwd, "shot", forward)
            total = add(total, fwd, order_arr[(pos - t) % n_shot])
        if t <= n_bwd:
            bwd = lax.ppermute(bwd, "shot", backward)
            total = add(total, bwd, order_arr[(pos + t) % n_shot])
    factor = (2.0 * APER * BLOCK) ** (-0.5)
    total = (total * factor).astype(jnp.bfloat16)
    return total.reshape(freqs, parts, shots_here, rcv_here)


def solution(mesh):
    n_shot = mesh.shape["shot"]
    n_rcv = mesh.shape["rcv"]
    placed = (P(None, None, "shot", "rcv"), P("shot", None), P(), P())

    def body(records, aperture, block_owner, block_receivers):
        return per_device(records, aperture, block_owner, block_receivers, n_shot, n_rcv)

    return jax.shard_map(
        body,
        mesh=mesh,
        in_specs=placed,
        out_specs=P(None, None, "shot", "rcv"),
        check_vma=False,
    )
```

```python
import jax
import jax.numpy as jnp
from jax import lax
from jax.sharding import PartitionSpec as P

APER = 2
BLOCK = 128


def ring_order(n):
    if n % 2:
        return list(range(n))
    return list(range(0, n, 2)) + list(range(n - 1, 0, -2))


def local_columns(records, block_receivers):
    rcv_here = records.shape[3]
    first_rcv = lax.axis_index("rcv") * rcv_here
    requested = block_receivers.reshape(1, -1)
    column_ids = first_rcv + lax.broadcasted_iota(jnp.int32, (rcv_here, 1), 0)
    selector = (column_ids == requested).astype(jnp.bfloat16)
    picked = jnp.einsum("fcsr,rx->fcsx", records, selector, preferred_element_type=jnp.float32)
    return picked.astype(jnp.bfloat16)


def gather_near(picked, n_rcv):
    total = picked.astype(jnp.float32)
    for k in range(1, n_rcv):
        moved = lax.ppermute(picked, "rcv", [(i, (i + k) % n_rcv) for i in range(n_rcv)])
        total = total + moved.astype(jnp.float32)
    return total.astype(jnp.bfloat16)


def piece_product(lhs, piece):
    nblk, freqs, parts, extent, width = piece.shape
    rhs = piece.transpose(1, 2, 0, 3, 4).reshape(freqs, parts * nblk * extent, width)
    return jnp.einsum("fsk,fkw->fsw", lhs, rhs, preferred_element_type=jnp.float32)


def per_device(records, aperture, block_owner, block_receivers, n_shot, n_rcv):
    freqs, parts, shots_here, rcv_here = records.shape
    nblocks, block_extent = block_receivers.shape

    picked = local_columns(records, block_receivers)
    near = gather_near(picked, n_rcv)
    blocks = lax.broadcasted_iota(jnp.int32, (1, 1, nblocks), 2)
    use = jnp.any(aperture[:, :, None] == blocks, axis=1).astype(jnp.bfloat16)
    masked = near.reshape(freqs, parts, shots_here, nblocks, block_extent) * use[None, None, :, :, None]
    masked = masked.reshape(freqs, parts, shots_here, nblocks * block_extent)
    nr, ni = masked[:, 0], masked[:, 1]
    lhs = jnp.concatenate(
        [jnp.concatenate([nr, -ni], axis=2), jnp.concatenate([ni, nr], axis=2)], axis=1
    )

    order = ring_order(n_shot)
    where = [0] * n_shot
    for k, d in enumerate(order):
        where[d] = k
    order_arr = jnp.array(order, jnp.int32)
    me = lax.axis_index("shot")
    pos = jnp.array(where, jnp.int32)[me]
    forward = [(order[k], order[(k + 1) % n_shot]) for k in range(n_shot)]
    backward = [(order[k], order[(k - 1) % n_shot]) for k in range(n_shot)]
    n_fwd = n_shot // 2
    n_bwd = n_shot - 1 - n_fwd

    rows = shots_here // n_shot
    split_last = n_fwd > n_bwd and rcv_here % 2 == 0
    half = rcv_here // 2
    nk = lhs.shape[2]
    lhs_rows = lhs.reshape(freqs, 2 * shots_here, nk // block_extent, block_extent)

    def add(total, piece, source):
        part = lax.dynamic_slice_in_dim(lhs_rows, source * rows, rows, axis=3)
        part = part.reshape(freqs, 2 * shots_here, -1)
        rhs = piece.transpose(1, 2, 0, 3, 4).reshape(freqs, -1, rcv_here)
        return total + jnp.einsum("fsk,fkw->fsw", part, rhs, preferred_element_type=jnp.float32)

    split = records.reshape(freqs, parts, n_shot, rows, rcv_here).transpose(2, 0, 1, 3, 4)
    pieces = lax.all_to_all(split, "shot", 0, 0, tiled=True)
    mine = jnp.take(pieces, block_owner, axis=0)

    total = add(jnp.zeros((freqs, 2 * shots_here, rcv_here), jnp.float32), mine, me)
    fwd, bwd = mine, mine
    for t in range(1, max(n_fwd, n_bwd) + 1):
        if t == n_fwd and split_last:
            first = lax.ppermute(fwd[..., :half], "shot", forward)
            second = lax.ppermute(bwd[..., half:], "shot", backward)
            joined = jnp.concatenate([first, second], axis=-1)
            total = add(total, joined, order_arr[(pos - t) % n_shot])
            continue
        if t <= n_fwd:
            fwd = lax.ppermute(fwd, "shot", forward)
            total = add(total, fwd, order_arr[(pos - t) % n_shot])
        if t <= n_bwd:
            bwd = lax.ppermute(bwd, "shot", backward)
            total = add(total, bwd, order_arr[(pos + t) % n_shot])
    factor = (2.0 * APER * BLOCK) ** (-0.5)
    total = (total * factor).astype(jnp.bfloat16)
    return total.reshape(freqs, parts, shots_here, rcv_here)


def solution(mesh):
    n_shot = mesh.shape["shot"]
    n_rcv = mesh.shape["rcv"]
    placed = (P(None, None, "shot", "rcv"), P("shot", None), P(), P())

    def body(records, aperture, block_owner, block_receivers):
        return per_device(records, aperture, block_owner, block_receivers, n_shot, n_rcv)

    return jax.shard_map(
        body,
        mesh=mesh,
        in_specs=placed,
        out_specs=P(None, None, "shot", "rcv"),
        check_vma=False,
    )
```
